128 devices in a mesh: ind: 32 (over z_hi, x, y), win: 4 (over z_lo, core).
Axes of the slice: x: 4, y: 4, z: 4 (z_hi: 2, z_lo: 2; z = z_hi * 2 + z_lo), core: 2. Of those that a mesh axis runs over, the one named last changes fastest.
Arguments:
- dosage: bfloat16 [65536, 4096], P('ind', 'win'), may hold values from 0 to 2
- tail: bfloat16 [65536, 512], P('ind'), may hold values from 0 to 2
- missing: int32 [4608], replicated, may hold values from 0 to 32767
- start: float32 [8, 1024, 8], P('win'), may hold values from -6 to 6
Outputs:
- loadings: float32 [8, 1024, 8], P('win')
- variances: float32 [8, 8], P('win')
- scores: float32 [65536, 8], P('ind', 'win')
The draws below stay inside these ranges and needn't reach their ends.
All inputs are finite; a program needn't handle non-finite values.
Results may differ from the reference program's by a relative error of at most 0.0024.
Values may be sent and summed in bfloat16 or wider, within the bound.
No kernel may reach another device: no remote copies, remote signals or barrier semaphores. Data moves between devices by JAX's collectives and lax.ppermute only.
A program may use at most 128 MiB of HBM per device.

```python
import jax
import jax.numpy as jnp
from jax import lax

W = 1024
HALF = 512
K = 8
ITERS = 6
INDS = 65536
SNPS = 4096
WINDOWS = 8


def set_ends(drawn, key, least, high):
    longest = drawn.shape.index(max(drawn.shape))
    spots = []
    for shift in (0, 1):
        where = [jax.random.randint(jax.random.fold_in(key, axis), (), 0, length) for axis, length in enumerate(drawn.shape)]
        where[longest] = (where[longest] + shift) % drawn.shape[longest]
        spots.append(tuple(where))
    return drawn.at[spots[0]].set(least).at[spots[1]].set(high)


def block_levels(rng, extent, split, smallest, high):
    def one(position, blocks):
        heights = jax.random.uniform(jax.random.fold_in(jax.random.fold_in(rng, 6), position), (blocks,), jnp.float32, smallest / len(split), high / len(split))
        return jnp.repeat(jnp.exp(heights), extent[position] // blocks).reshape((-1,) + (1,) * (len(extent) - position - 1))

    gain = one(*split[0])
    for cut in split[1:]:
        gain = gain * one(*cut)
    return gain


def noise(own_key, dims, spread, limit, pieces=(), dtype=jnp.bfloat16):
    gain = block_levels(own_key, dims, pieces, -0.22, 0.18) if pieces else 1.0
    drawn = jax.random.normal(own_key, dims, jnp.float32) * spread * gain
    return jnp.minimum(jnp.maximum(drawn, -limit), limit).astype(dtype)


def setup_inputs(seed: int = 0) -> dict:
    splits = jax.random.split(jax.random.key(seed), 5)
    return {
        "dosage": jnp.clip(2.0 * jax.random.uniform(splits[0], (INDS, SNPS), jnp.float32) ** block_levels(splits[0], (INDS, SNPS), ((0, 32), (1, 4)), -0.2, 0.2), 0.0, 2.0).astype(jnp.bfloat16),
        "tail": jnp.clip(2.0 * jax.random.uniform(splits[1], (INDS, HALF), jnp.float32) ** block_levels(splits[1], (INDS, HALF), ((0, 32),), -0.2, 0.2), 0.0, 2.0).astype(jnp.bfloat16),
        "missing": set_ends(jax.random.randint(splits[2], (SNPS + HALF,), 0, INDS // 2), jax.random.fold_in(splits[2], 1), 0, (INDS // 2) - 1).astype(jnp.int32),
        "start": noise(splits[3], (WINDOWS, W, K), 1.0, 6.0, ((0, 4),), jnp.float32),
    }


def orthonormal(image):
    gram = jnp.dot(image.T, image, precision=lax.Precision.HIGHEST)
    factor = jnp.linalg.cholesky(gram)
    solved = jax.scipy.linalg.solve_triangular(factor, image.T, lower=True)
    return solved.T

def reference(dosage, tail, missing, start):
    region = jnp.concatenate([dosage, tail], axis=1).astype(jnp.float32)
    total = region.shape[0]
    mean = lax.optimization_barrier(jnp.sum(region, axis=0)) / total
    var = lax.optimization_barrier(jnp.sum(region * region, axis=0)) / total - mean * mean
    weight = jnp.sqrt((total - missing.astype(jnp.float32)) / total)
    stand = ((region - mean) / jnp.sqrt(var + 1e-05) * weight).astype(jnp.bfloat16)
    width = start.shape[1]
    half_cols = width // 2
    loads = []
    varis = []
    scorelist = []
    for window in range(start.shape[0]):
        block = stand[:, window * half_cols:window * half_cols + width]
        cov = jnp.dot(block.T.astype(jnp.float32), block.astype(jnp.float32), preferred_element_type=jnp.float32) / total
        basis = start[window]
        for step in range(ITERS):
            basis = orthonormal(jnp.dot(cov, basis, precision=lax.Precision.HIGHEST))
        image = jnp.dot(cov, basis, precision=lax.Precision.HIGHEST)
        varis.append(lax.optimization_barrier(jnp.sum(basis * image, axis=0)))
        loads.append(basis)
        blockf = block.astype(jnp.float32)
        proj = jnp.dot(blockf, basis, precision=lax.Precision.HIGHEST)
        rest = blockf - jnp.dot(proj, basis.T, precision=lax.Precision.HIGHEST)
        scorelist.append(lax.optimization_barrier(jnp.sum(rest * rest, axis=1)) / width)
    return (jnp.stack(loads, 0), jnp.stack(varis, 0), jnp.stack(scorelist, 1))
```

```python
import jax
import jax.numpy as jnp
from jax import lax
from jax.sharding import PartitionSpec as P

ITERS = 6
HIGHEST = lax.Precision.HIGHEST


def passed_along(array, axis, by):
    size = lax.axis_size(axis)
    pairs = [(i, i + by) for i in range(size) if 0 <= i + by < size]
    return lax.ppermute(array, axis, pairs)


def swapped(value, axis, mask):
    size = lax.axis_size(axis)
    return lax.ppermute(value, axis, [(i, i ^ mask) for i in range(size)])


def summed(value, axis):
    size = lax.axis_size(axis)
    if size & (size - 1):
        return lax.psum(value, axis)
    bit = 1
    while bit < size:
        if bit * 4 <= size:
            near = swapped(value, axis, bit)
            mid = swapped(value, axis, 2 * bit)
            far = swapped(value, axis, 3 * bit)
            value = (value + near) + (mid + far)
            bit *= 4
        else:
            value = value + swapped(value, axis, bit)
            bit *= 2
    return value


def orthonormal(image):
    gram = jnp.einsum("swk,swl->skl", image, image, precision=HIGHEST)
    factor = jnp.linalg.cholesky(gram)
    solved = jax.vmap(lambda fac, rhs: jax.scipy.linalg.solve_triangular(fac, rhs, lower=True))(
        factor, jnp.swapaxes(image, 1, 2)
    )
    return jnp.swapaxes(solved, 1, 2)


def widened(basis, half_cols):
    pad = jnp.zeros((half_cols, basis.shape[2]), basis.dtype)
    first = jnp.concatenate([basis[0], pad], axis=0)
    second = jnp.concatenate([pad, basis[1]], axis=0)
    return jnp.concatenate([first, second], axis=1)


def shards(dosage, tail, missing, start):
    win_count = lax.axis_size("win")
    position = lax.axis_index("win")
    columns = dosage.shape[1]
    half_cols = columns // 2
    comps = start.shape[2]
    total = dosage.shape[0] * lax.axis_size("ind")
    received = passed_along(dosage[:, :half_cols], "win", -1)
    following = jnp.where(position == win_count - 1, tail, received)
    region = jnp.concatenate([dosage, following], axis=1)
    regionf = region.astype(jnp.float32)
    stats = summed(jnp.stack([jnp.sum(regionf, axis=0), jnp.sum(regionf * regionf, axis=0)]), "ind")
    mean = stats[0] / total
    var = stats[1] / total - mean * mean
    miss_here = lax.dynamic_slice_in_dim(missing, position * columns, columns + half_cols)
    weight = jnp.sqrt((total - miss_here.astype(jnp.float32)) / total)
    stand = ((regionf - mean) / jnp.sqrt(var + 1e-05) * weight).astype(jnp.bfloat16)
    standf = stand.astype(jnp.float32)

    def project(basis):
        return jnp.dot(standf, widened(basis, half_cols), precision=HIGHEST)

    def image_of(basis):
        proj = project(basis)
        back = lax.dot_general(standf, proj, (((0,), (0,)), ((), ())), precision=HIGHEST)
        parts = jnp.stack([back[:columns, :comps], back[half_cols:, comps:]], 0)
        return summed(parts, "ind") / total

    basis = start
    for step in range(ITERS):
        basis = orthonormal(image_of(basis))
    proj = project(basis)
    variances = summed(jnp.sum(proj * proj, axis=0), "ind").reshape(2, comps) / total
    first = standf[:, :columns] - jnp.dot(proj[:, :comps], basis[0].T, precision=HIGHEST)
    second = standf[:, half_cols:] - jnp.dot(proj[:, comps:], basis[1].T, precision=HIGHEST)
    scores = jnp.stack([jnp.sum(first * first, axis=1), jnp.sum(second * second, axis=1)], 1) / columns
    return (basis, variances, scores)


def solution(mesh):
    in_specs = (P("ind", "win"), P("ind", None), P(), P("win", None, None))
    out_specs = (P("win", None, None), P("win", None), P("ind", "win"))
    return jax.shard_map(shards, mesh=mesh, in_specs=in_specs, out_specs=out_specs, check_vma=False)
```

```python
import jax
import jax.numpy as jnp
from jax import lax
from jax.sharding import PartitionSpec as P

ITERS = 6
HIGHEST = lax.Precision.HIGHEST


def passed_along(array, axis, by):
    size = lax.axis_size(axis)
    pairs = [(i, i + by) for i in range(size) if 0 <= i + by < size]
    return lax.ppermute(array, axis, pairs)


def swapped(value, axis, mask):
    size = lax.axis_size(axis)
    return lax.ppermute(value, axis, [(i, i ^ mask) for i in range(size)])


def summed(value, axis):
    size = lax.axis_size(axis)
    if size & (size - 1):
        return lax.psum(value, axis)
    bit = 1
    while bit < size:
        if bit * 4 <= size:
            near = swapped(value, axis, bit)
            mid = swapped(value, axis, 2 * bit)
            far = swapped(value, axis, 3 * bit)
            value = (value + near) + (mid + far)
            bit *= 4
        else:
            value = value + swapped(value, axis, bit)
            bit *= 2
    return value


def orthonormal(image):
    gram = jnp.einsum("swk,swl->skl", image, image, precision=HIGHEST)
    factor = jnp.linalg.cholesky(gram)
    solved = jax.vmap(lambda fac, rhs: jax.scipy.linalg.solve_triangular(fac, rhs, lower=True))(
        factor, jnp.swapaxes(image, 1, 2)
    )
    return jnp.swapaxes(solved, 1, 2)


def pieces(value):
    high = lax.reduce_precision(value, exponent_bits=8, mantissa_bits=7)
    rest = value - high
    mid = lax.reduce_precision(rest, exponent_bits=8, mantissa_bits=7)
    low = rest - mid
    return high.astype(jnp.bfloat16), mid.astype(jnp.bfloat16), low.astype(jnp.bfloat16)


def thirds(value):
    width = value.shape[1] // 3
    return (value[:, :width] + value[:, width : 2 * width]) + value[:, 2 * width :]


def product(left, right):
    l1, l2, l3 = pieces(left)
    r1, r2, r3 = pieces(right)
    lhs = jnp.concatenate([l1, l1, l2, l1, l2, l3], 1)
    rhs = jnp.concatenate([r1, r2, r1, r3, r2, r1], 1)
    return lax.dot_general(lhs, rhs, (((1,), (1,)), ((), ())), preferred_element_type=jnp.float32)


def widened(basis, half_cols):
    pad = jnp.zeros((half_cols, basis.shape[2]), basis.dtype)
    first = jnp.concatenate([basis[0], pad], axis=0)
    second = jnp.concatenate([pad, basis[1]], axis=0)
    return jnp.concatenate([first, second], axis=1)


def shards(dosage, tail, missing, start):
    win_count = lax.axis_size("win")
    position = lax.axis_index("win")
    columns = dosage.shape[1]
    half_cols = columns // 2
    comps = start.shape[2]
    total = dosage.shape[0] * lax.axis_size("ind")
    received = passed_along(dosage[:, :half_cols], "win", -1)
    following = jnp.where(position == win_count - 1, tail, received)
    region = jnp.concatenate([dosage, following], axis=1)
    regionf = region.astype(jnp.float32)
    stats = summed(jnp.stack([jnp.sum(regionf, axis=0), jnp.sum(regionf * regionf, axis=0)]), "ind")
    mean = stats[0] / total
    var = stats[1] / total - mean * mean
    miss_here = lax.dynamic_slice_in_dim(missing, position * columns, columns + half_cols)
    weight = jnp.sqrt((total - miss_here.astype(jnp.float32)) / total)
    stand = ((regionf - mean) / jnp.sqrt(var + 1e-05) * weight).astype(jnp.bfloat16)
    standf = stand.astype(jnp.float32)

    def project(basis):
        wide = widened(basis, half_cols)
        return thirds(jnp.dot(stand, jnp.concatenate(pieces(wide), 1), preferred_element_type=jnp.float32))

    def image_of(basis):
        proj = project(basis)
        split = jnp.concatenate(pieces(proj), 1)
        back = thirds(lax.dot_general(stand, split, (((0,), (0,)), ((), ())), preferred_element_type=jnp.float32))
        parts = jnp.stack([back[:columns, :comps], back[half_cols:, comps:]], 0)
        return summed(parts, "ind") / total

    basis = start
    for step in range(ITERS):
        basis = orthonormal(image_of(basis))
    proj = project(basis)
    variances = summed(jnp.sum(proj * proj, axis=0), "ind").reshape(2, comps) / total
    first = standf[:, :columns] - product(proj[:, :comps], basis[0])
    second = standf[:, half_cols:] - product(proj[:, comps:], basis[1])
    scores = jnp.stack([jnp.sum(first * first, axis=1), jnp.sum(second * second, axis=1)], 1) / columns
    return (basis, variances, scores)


def solution(mesh):
    in_specs = (P("ind", "win"), P("ind", None), P(), P("win", None, None))
    out_specs = (P("win", None, None), P("win", None), P("ind", "win"))
    return jax.shard_map(shards, mesh=mesh, in_specs=in_specs, out_specs=out_specs, check_vma=False)
```

```python
import jax
import jax.numpy as jnp
from jax import lax
from jax.sharding import PartitionSpec as P

ITERS = 6
HIGHEST = lax.Precision.HIGHEST


def passed_along(array, axis, by):
    size = lax.axis_size(axis)
    pairs = [(i, i + by) for i in range(size) if 0 <= i + by < size]
    return lax.ppermute(array, axis, pairs)


def swapped(value, axis, mask):
    size = lax.axis_size(axis)
    return lax.ppermute(value, axis, [(i, i ^ mask) for i in range(size)])


def summed(value, axis):
    size = lax.axis_size(axis)
    if size & (size - 1):
        return lax.psum(value, axis)
    bit = 1
    while bit < size:
        value = value + swapped(value, axis, bit)
        bit *= 2
    return value


def orthonormal(image):
    gram = jnp.einsum("swk,swl->skl", image, image, precision=HIGHEST)
    factor = jnp.linalg.cholesky(gram)
    solved = jax.vmap(lambda fac, rhs: jax.scipy.linalg.solve_triangular(fac, rhs, lower=True))(
        factor, jnp.swapaxes(image, 1, 2)
    )
    return jnp.swapaxes(solved, 1, 2)


def pieces(value):
    high = lax.reduce_precision(value, exponent_bits=8, mantissa_bits=7)
    rest = value - high
    mid = lax.reduce_precision(rest, exponent_bits=8, mantissa_bits=7)
    low = rest - mid
    return high.astype(jnp.bfloat16), mid.astype(jnp.bfloat16), low.astype(jnp.bfloat16)


def thirds(value):
    width = value.shape[1] // 3
    return (value[:, :width] + value[:, width : 2 * width]) + value[:, 2 * width :]


def product(left, right):
    l1, l2, l3 = pieces(left)
    r1, r2, r3 = pieces(right)
    lhs = jnp.concatenate([l1, l1, l2, l1, l2, l3], 1)
    rhs = jnp.concatenate([r1, r2, r1, r3, r2, r1], 1)
    return lax.dot_general(lhs, rhs, (((1,), (1,)), ((), ())), preferred_element_type=jnp.float32)


def widened(basis, half_cols):
    pad = jnp.zeros((half_cols, basis.shape[2]), basis.dtype)
    first = jnp.concatenate([basis[0], pad], axis=0)
    second = jnp.concatenate([pad, basis[1]], axis=0)
    return jnp.concatenate([first, second], axis=1)


def shards(dosage, tail, missing, start):
    win_count = lax.axis_size("win")
    position = lax.axis_index("win")
    columns = dosage.shape[1]
    half_cols = columns // 2
    comps = start.shape[2]
    total = dosage.shape[0] * lax.axis_size("ind")
    received = passed_along(dosage[:, :half_cols], "win", -1)
    following = jnp.where(position == win_count - 1, tail, received)
    region = jnp.concatenate([dosage, following], axis=1)
    regionf = region.astype(jnp.float32)
    stats = summed(jnp.stack([jnp.sum(regionf, axis=0), jnp.sum(regionf * regionf, axis=0)]), "ind")
    mean = stats[0] / total
    var = stats[1] / total - mean * mean
    miss_here = lax.dynamic_slice_in_dim(missing, position * columns, columns + half_cols)
    weight = jnp.sqrt((total - miss_here.astype(jnp.float32)) / total)
    stand = ((regionf - mean) / jnp.sqrt(var + 1e-05) * weight).astype(jnp.bfloat16)
    standf = stand.astype(jnp.float32)

    def project(basis):
        wide = widened(basis, half_cols)
        return thirds(jnp.dot(stand, jnp.concatenate(pieces(wide), 1), preferred_element_type=jnp.float32))

    def image_of(basis):
        proj = project(basis)
        split = jnp.concatenate(pieces(proj), 1)
        back = thirds(lax.dot_general(stand, split, (((0,), (0,)), ((), ())), preferred_element_type=jnp.float32))
        parts = jnp.stack([back[:columns, :comps], back[half_cols:, comps:]], 0)
        return summed(parts, "ind") / total

    basis = start
    for step in range(ITERS):
        basis = orthonormal(image_of(basis))
    proj = project(basis)
    variances = summed(jnp.sum(proj * proj, axis=0), "ind").reshape(2, comps) / total
    first = standf[:, :columns] - product(proj[:, :comps], basis[0])
    second = standf[:, half_cols:] - product(proj[:, comps:], basis[1])
    scores = jnp.stack([jnp.sum(first * first, axis=1), jnp.sum(second * second, axis=1)], 1) / columns
    return (basis, variances, scores)


def solution(mesh):
    in_specs = (P("ind", "win"), P("ind", None), P(), P("win", None, None))
    out_specs = (P("win", None, None), P("win", None), P("ind", "win"))
    return jax.shard_map(shards, mesh=mesh, in_specs=in_specs, out_specs=out_specs, check_vma=False)
```

```python
import jax
import jax.numpy as jnp
from jax import lax
from jax.sharding import PartitionSpec as P

ITERS = 6
HIGHEST = lax.Precision.HIGHEST


def passed_along(array, axis, by):
    size = lax.axis_size(axis)
    pairs = [(i, i + by) for i in range(size) if 0 <= i + by < size]
    return lax.ppermute(array, axis, pairs)


def swapped(value, axis, mask):
    size = lax.axis_size(axis)
    return lax.ppermute(value, axis, [(i, i ^ mask) for i in range(size)])


def summed(value, axis):
    size = lax.axis_size(axis)
    if size & (size - 1):
        return lax.psum(value, axis)
    bit = 1
    while bit < size:
        if bit * 4 <= size:
            near = swapped(value, axis, bit)
            mid = swapped(value, axis, 2 * bit)
            far = swapped(value, axis, 3 * bit)
            value = (value + near) + (mid + far)
            bit *= 4
        else:
            value = value + swapped(value, axis, bit)
            bit *= 2
    return value


def orthonormal(image):
    gram = jnp.einsum("swk,swl->skl", image, image, precision=HIGHEST)
    factor = jnp.linalg.cholesky(gram)
    solved = jax.vmap(lambda fac, rhs: jax.scipy.linalg.solve_triangular(fac, rhs, lower=True))(
        factor, jnp.swapaxes(image, 1, 2)
    )
    return jnp.swapaxes(solved, 1, 2)


def pieces(value):
    high = lax.reduce_precision(value, exponent_bits=8, mantissa_bits=7)
    rest = value - high
    mid = lax.reduce_precision(rest, exponent_bits=8, mantissa_bits=7)
    low = rest - mid
    return high.astype(jnp.bfloat16), mid.astype(jnp.bfloat16), low.astype(jnp.bfloat16)


def thirds(value):
    width = value.shape[1] // 3
    return (value[:, :width] + value[:, width : 2 * width]) + value[:, 2 * width :]


def product(left, right):
    l1, l2, l3 = pieces(left)
    r1, r2, r3 = pieces(right)
    lhs = jnp.concatenate([l1, l1, l2, l1, l2, l3], 1)
    rhs = jnp.concatenate([r1, r2, r1, r3, r2, r1], 1)
    return lax.dot_general(lhs, rhs, (((1,), (1,)), ((), ())), preferred_element_type=jnp.float32)


def widened(basis, half_cols):
    pad = jnp.zeros((half_cols, basis.shape[2]), basis.dtype)
    first = jnp.concatenate([basis[0], pad], axis=0)
    second = jnp.concatenate([pad, basis[1]], axis=0)
    return jnp.concatenate([first, second], axis=1)


def shards(dosage, tail, missing, start):
    win_count = lax.axis_size("win")
    position = lax.axis_index("win")
    columns = dosage.shape[1]
    half_cols = columns // 2
    comps = start.shape[2]
    total = dosage.shape[0] * lax.axis_size("ind")
    received = passed_along(dosage[:, :half_cols], "win", -1)
    following = jnp.where(position == win_count - 1, tail, received)
    region = jnp.concatenate([dosage, following], axis=1)
    regionf = region.astype(jnp.float32)
    stats = summed(jnp.stack([jnp.sum(regionf, axis=0), jnp.sum(regionf * regionf, axis=0)]), "ind")
    mean = stats[0] / total
    var = stats[1] / total - mean * mean
    miss_here = lax.dynamic_slice_in_dim(missing, position * columns, columns + half_cols)
    weight = jnp.sqrt((total - miss_here.astype(jnp.float32)) / total)
    stand = ((regionf - mean) / jnp.sqrt(var + 1e-05) * weight).astype(jnp.bfloat16)
    standf = stand.astype(jnp.float32)

    def project(basis):
        wide = widened(basis, half_cols)
        return thirds(jnp.dot(stand, jnp.concatenate(pieces(wide), 1), preferred_element_type=jnp.float32))

    def image_of(basis):
        proj = project(basis)
        split = jnp.concatenate(pieces(proj), 1)
        back = thirds(lax.dot_general(stand, split, (((0,), (0,)), ((), ())), preferred_element_type=jnp.float32))
        parts = jnp.stack([back[:columns, :comps], back[half_cols:, comps:]], 0)
        return summed(parts, "ind") / total

    basis = lax.fori_loop(0, ITERS, lambda step, basis: orthonormal(image_of(basis)), start)
    proj = project(basis)
    variances = summed(jnp.sum(proj * proj, axis=0), "ind").reshape(2, comps) / total
    first = standf[:, :columns] - product(proj[:, :comps], basis[0])
    second = standf[:, half_cols:] - product(proj[:, comps:], basis[1])
    scores = jnp.stack([jnp.sum(first * first, axis=1), jnp.sum(second * second, axis=1)], 1) / columns
    return (basis, variances, scores)


def solution(mesh):
    in_specs = (P("ind", "win"), P("ind", None), P(), P("win", None, None))
    out_specs = (P("win", None, None), P("win", None), P("ind", "win"))
    return jax.shard_map(shards, mesh=mesh, in_specs=in_specs, out_specs=out_specs, check_vma=False)
```

```python
import jax
import jax.numpy as jnp
from jax import lax
from jax.sharding import PartitionSpec as P

ITERS = 6
HIGHEST = lax.Precision.HIGHEST


def passed_along(array, axis, by):
    size = lax.axis_size(axis)
    pairs = [(i, i + by) for i in range(size) if 0 <= i + by < size]
    return lax.ppermute(array, axis, pairs)


def swapped(value, axis, mask):
    size = lax.axis_size(axis)
    return lax.ppermute(value, axis, [(i, i ^ mask) for i in range(size)])


def summed(value, axis):
    size = lax.axis_size(axis)
    if size & (size - 1):
        return lax.psum(value, axis)
    bit = 1
    while bit < size:
        if bit * 4 <= size:
            near = swapped(value, axis, bit)
            mid = swapped(value, axis, 2 * bit)
            far = swapped(value, axis, 3 * bit)
            value = (value + near) + (mid + far)
            bit *= 4
        else:
            value = value + swapped(value, axis, bit)
            bit *= 2
    return value


def orthonormal(image):
    gram = jnp.einsum("swk,swl->skl", image, image, precision=HIGHEST)
    factor = jnp.linalg.cholesky(gram)
    solved = jax.vmap(lambda fac, rhs: jax.scipy.linalg.solve_triangular(fac, rhs, lower=True))(
        factor, jnp.swapaxes(image, 1, 2)
    )
    return jnp.swapaxes(solved, 1, 2)


def pieces(value):
    high = lax.reduce_precision(value, exponent_bits=8, mantissa_bits=7)
    rest = value - high
    mid = lax.reduce_precision(rest, exponent_bits=8, mantissa_bits=7)
    low = rest - mid
    return high.astype(jnp.bfloat16), mid.astype(jnp.bfloat16), low.astype(jnp.bfloat16)


def thirds(value):
    width = value.shape[1] // 3
    return (value[:, :width] + value[:, width : 2 * width]) + value[:, 2 * width :]


def product(left, right):
    l1, l2, l3 = pieces(left)
    r1, r2, r3 = pieces(right)
    lhs = jnp.concatenate([l1, l1, l2, l1, l2, l3], 1)
    rhs = jnp.concatenate([r1, r2, r1, r3, r2, r1], 1)
    return lax.dot_general(lhs, rhs, (((1,), (1,)), ((), ())), preferred_element_type=jnp.float32)


def widened(basis, half_cols):
    pad = jnp.zeros((half_cols, basis.shape[2]), basis.dtype)
    first = jnp.concatenate([basis[0], pad], axis=0)
    second = jnp.concatenate([pad, basis[1]], axis=0)
    return jnp.concatenate([first, second], axis=1)


def shards(dosage, tail, missing, start):
    win_count = lax.axis_size("win")
    position = lax.axis_index("win")
    columns = dosage.shape[1]
    half_cols = columns // 2
    comps = start.shape[2]
    total = dosage.shape[0] * lax.axis_size("ind")
    received = passed_along(dosage[:, :half_cols], "win", -1)
    following = jnp.where(position == win_count - 1, tail, received)
    region = jnp.concatenate([dosage, following], axis=1)
    regionf = region.astype(jnp.float32)
    stats = summed(jnp.stack([jnp.sum(regionf, axis=0), jnp.sum(regionf * regionf, axis=0)]), "ind")
    mean = stats[0] / total
    var = stats[1] / total - mean * mean
    miss_here = lax.dynamic_slice_in_dim(missing, position * columns, columns + half_cols)
    weight = jnp.sqrt((total - miss_here.astype(jnp.float32)) / total)
    stand = ((regionf - mean) / jnp.sqrt(var + 1e-05) * weight).astype(jnp.bfloat16)

    def project(basis):
        wide = widened(basis, half_cols)
        return thirds(jnp.dot(stand, jnp.concatenate(pieces(wide), 1), preferred_element_type=jnp.float32))

    def image_of(basis):
        proj = project(basis)
        split = jnp.concatenate(pieces(proj), 1)
        back = thirds(lax.dot_general(stand, split, (((0,), (0,)), ((), ())), preferred_element_type=jnp.float32))
        parts = jnp.stack([back[:columns, :comps], back[half_cols:, comps:]], 0)
        return summed(parts, "ind") / total

    basis = lax.fori_loop(0, ITERS, lambda step, basis: orthonormal(image_of(basis)), start)
    proj = project(basis)
    variances = summed(jnp.sum(proj * proj, axis=0), "ind").reshape(2, comps) / total
    first = stand[:, :columns].astype(jnp.float32) - product(proj[:, :comps], basis[0])
    second = stand[:, half_cols:].astype(jnp.float32) - product(proj[:, comps:], basis[1])
    scores = jnp.stack([jnp.sum(first * first, axis=1), jnp.sum(second * second, axis=1)], 1) / columns
    return (basis, variances, scores)


def solution(mesh):
    in_specs = (P("ind", "win"), P("ind", None), P(), P("win", None, None))
    out_specs = (P("win", None, None), P("win", None), P("ind", "win"))
    return jax.shard_map(shards, mesh=mesh, in_specs=in_specs, out_specs=out_specs, check_vma=False)
```

```python
import jax
import jax.numpy as jnp
from jax import lax
from jax.sharding import PartitionSpec as P

ITERS = 6
HIGHEST = lax.Precision.HIGHEST


def passed_along(array, axis, by):
    size = lax.axis_size(axis)
    pairs = [(i, i + by) for i in range(size) if 0 <= i + by < size]
    return lax.ppermute(array, axis, pairs)


def swapped(value, axis, mask):
    size = lax.axis_size(axis)
    return lax.ppermute(value, axis, [(i, i ^ mask) for i in range(size)])


def summed(value, axis):
    size = lax.axis_size(axis)
    if size & (size - 1):
        return lax.psum(value, axis)
    bit = 1
    while bit < size:
        group = 8 if bit * 8 <= size and bit > 1 else min(4, size // bit)
        got = [value] + [swapped(value, axis, bit * offset) for offset in range(1, group)]
        while len(got) > 1:
            got = [got[i] + got[i + 1] for i in range(0, len(got), 2)]
        value = got[0]
        bit *= group
    return value


def orthonormal(image):
    gram = jnp.einsum("swk,swl->skl", image, image, precision=HIGHEST)
    factor = jnp.linalg.cholesky(gram)
    solved = jax.vmap(lambda fac, rhs: jax.scipy.linalg.solve_triangular(fac, rhs, lower=True))(
        factor, jnp.swapaxes(image, 1, 2)
    )
    return jnp.swapaxes(solved, 1, 2)


def pieces(value):
    high = lax.reduce_precision(value, exponent_bits=8, mantissa_bits=7)
    rest = value - high
    mid = lax.reduce_precision(rest, exponent_bits=8, mantissa_bits=7)
    low = rest - mid
    return high.astype(jnp.bfloat16), mid.astype(jnp.bfloat16), low.astype(jnp.bfloat16)


def thirds(value):
    width = value.shape[1] // 3
    return (value[:, :width] + value[:, width : 2 * width]) + value[:, 2 * width :]


def product(left, right):
    l1, l2, l3 = pieces(left)
    r1, r2, r3 = pieces(right)
    lhs = jnp.concatenate([l1, l1, l2, l1, l2, l3], 1)
    rhs = jnp.concatenate([r1, r2, r1, r3, r2, r1], 1)
    return lax.dot_general(lhs, rhs, (((1,), (1,)), ((), ())), preferred_element_type=jnp.float32)


def widened(basis, half_cols):
    pad = jnp.zeros((half_cols, basis.shape[2]), basis.dtype)
    first = jnp.concatenate([basis[0], pad], axis=0)
    second = jnp.concatenate([pad, basis[1]], axis=0)
    return jnp.concatenate([first, second], axis=1)


def shards(dosage, tail, missing, start):
    win_count = lax.axis_size("win")
    position = lax.axis_index("win")
    columns = dosage.shape[1]
    half_cols = columns // 2
    comps = start.shape[2]
    total = dosage.shape[0] * lax.axis_size("ind")
    received = passed_along(dosage[:, :half_cols], "win", -1)
    following = jnp.where(position == win_count - 1, tail, received)
    region = jnp.concatenate([dosage, following], axis=1)
    regionf = region.astype(jnp.float32)
    stats = summed(jnp.stack([jnp.sum(regionf, axis=0), jnp.sum(regionf * regionf, axis=0)]), "ind")
    mean = stats[0] / total
    var = stats[1] / total - mean * mean
    miss_here = lax.dynamic_slice_in_dim(missing, position * columns, columns + half_cols)
    weight = jnp.sqrt((total - miss_here.astype(jnp.float32)) / total)
    stand = ((regionf - mean) / jnp.sqrt(var + 1e-05) * weight).astype(jnp.bfloat16)

    def project(basis):
        wide = widened(basis, half_cols)
        return thirds(jnp.dot(stand, jnp.concatenate(pieces(wide), 1), preferred_element_type=jnp.float32))

    def image_of(basis):
        proj = project(basis)
        split = jnp.concatenate(pieces(proj), 1)
        back = thirds(lax.dot_general(stand, split, (((0,), (0,)), ((), ())), preferred_element_type=jnp.float32))
        parts = jnp.stack([back[:columns, :comps], back[half_cols:, comps:]], 0)
        return summed(parts, "ind") / total

    basis = lax.fori_loop(0, ITERS, lambda step, basis: orthonormal(image_of(basis)), start)
    proj = project(basis)
    variances = summed(jnp.sum(proj * proj, axis=0), "ind").reshape(2, comps) / total
    first = stand[:, :columns].astype(jnp.float32) - product(proj[:, :comps], basis[0])
    second = stand[:, half_cols:].astype(jnp.float32) - product(proj[:, comps:], basis[1])
    scores = jnp.stack([jnp.sum(first * first, axis=1), jnp.sum(second * second, axis=1)], 1) / columns
    return (basis, variances, scores)


def solution(mesh):
    in_specs = (P("ind", "win"), P("ind", None), P(), P("win", None, None))
    out_specs = (P("win", None, None), P("win", None), P("ind", "win"))
    return jax.shard_map(shards, mesh=mesh, in_specs=in_specs, out_specs=out_specs, check_vma=False)
```

```python
import jax
import jax.numpy as jnp
from jax import lax
from jax.experimental.layout import Layout, with_layout_constraint
from jax.sharding import PartitionSpec as P

ITERS = 6
HIGHEST = lax.Precision.HIGHEST


def passed_along(array, axis, by):
    size = lax.axis_size(axis)
    pairs = [(i, i + by) for i in range(size) if 0 <= i + by < size]
    return lax.ppermute(array, axis, pairs)


def swapped(value, axis, mask):
    size = lax.axis_size(axis)
    return lax.ppermute(value, axis, [(i, i ^ mask) for i in range(size)])


def summed(value, axis):
    size = lax.axis_size(axis)
    if size & (size - 1):
        return lax.psum(value, axis)
    bit = 1
    while bit < size:
        if bit * 4 <= size:
            near = swapped(value, axis, bit)
            mid = swapped(value, axis, 2 * bit)
            far = swapped(value, axis, 3 * bit)
            value = (value + near) + (mid + far)
            bit *= 4
        else:
            value = value + swapped(value, axis, bit)
            bit *= 2
    return value


def orthonormal(image):
    gram = jnp.einsum("swk,swl->skl", image, image, precision=HIGHEST)
    factor = jnp.linalg.cholesky(gram)
    solved = jax.vmap(lambda fac, rhs: jax.scipy.linalg.solve_triangular(fac, rhs, lower=True))(
        factor, jnp.swapaxes(image, 1, 2)
    )
    return jnp.swapaxes(solved, 1, 2)


def pieces(value):
    high = lax.reduce_precision(value, exponent_bits=8, mantissa_bits=7)
    rest = value - high
    mid = lax.reduce_precision(rest, exponent_bits=8, mantissa_bits=7)
    low = rest - mid
    return high.astype(jnp.bfloat16), mid.astype(jnp.bfloat16), low.astype(jnp.bfloat16)


def thirds(value):
    width = value.shape[1] // 3
    return (value[:, :width] + value[:, width : 2 * width]) + value[:, 2 * width :]


def product(left, right):
    l1, l2, l3 = pieces(left)
    r1, r2, r3 = pieces(right)
    lhs = jnp.concatenate([l1, l1, l2, l1, l2, l3], 1)
    rhs = jnp.concatenate([r1, r2, r1, r3, r2, r1], 1)
    return lax.dot_general(lhs, rhs, (((1,), (1,)), ((), ())), preferred_element_type=jnp.float32)


def widened(basis, half_cols):
    pad = jnp.zeros((half_cols, basis.shape[2]), basis.dtype)
    first = jnp.concatenate([basis[0], pad], axis=0)
    second = jnp.concatenate([pad, basis[1]], axis=0)
    return jnp.concatenate([first, second], axis=1)


def shards(dosage, tail, missing, start):
    win_count = lax.axis_size("win")
    position = lax.axis_index("win")
    columns = dosage.shape[1]
    half_cols = columns // 2
    comps = start.shape[2]
    total = dosage.shape[0] * lax.axis_size("ind")
    received = passed_along(dosage[:, :half_cols], "win", -1)
    following = jnp.where(position == win_count - 1, tail, received)
    region = jnp.concatenate([dosage, following], axis=1)
    regionf = region.astype(jnp.float32)
    stats = summed(jnp.stack([jnp.sum(regionf, axis=0), jnp.sum(regionf * regionf, axis=0)]), "ind")
    mean = stats[0] / total
    var = stats[1] / total - mean * mean
    miss_here = lax.dynamic_slice_in_dim(missing, position * columns, columns + half_cols)
    weight = jnp.sqrt((total - miss_here.astype(jnp.float32)) / total)
    stand = ((regionf - mean) / jnp.sqrt(var + 1e-05) * weight).astype(jnp.bfloat16)
    stand = with_layout_constraint(stand, Layout(major_to_minor=(0, 1)))

    def project(basis):
        wide = widened(basis, half_cols)
        return thirds(jnp.dot(stand, jnp.concatenate(pieces(wide), 1), preferred_element_type=jnp.float32))

    def image_of(basis):
        proj = project(basis)
        split = jnp.concatenate(pieces(proj), 1)
        back = thirds(lax.dot_general(stand, split, (((0,), (0,)), ((), ())), preferred_element_type=jnp.float32))
        parts = jnp.stack([back[:columns, :comps], back[half_cols:, comps:]], 0)
        return summed(parts, "ind") / total

    basis = lax.fori_loop(0, ITERS, lambda step, basis: orthonormal(image_of(basis)), start)
    proj = project(basis)
    variances = summed(jnp.sum(proj * proj, axis=0), "ind").reshape(2, comps) / total
    first = stand[:, :columns].astype(jnp.float32) - product(proj[:, :comps], basis[0])
    second = stand[:, half_cols:].astype(jnp.float32) - product(proj[:, comps:], basis[1])
    scores = jnp.stack([jnp.sum(first * first, axis=1), jnp.sum(second * second, axis=1)], 1) / columns
    return (basis, variances, scores)


def solution(mesh):
    in_specs = (P("ind", "win"), P("ind", None), P(), P("win", None, None))
    out_specs = (P("win", None, None), P("win", None), P("ind", "win"))
    return jax.shard_map(shards, mesh=mesh, in_specs=in_specs, out_specs=out_specs, check_vma=False)
```

```python
import jax
import jax.numpy as jnp
from jax import lax
from jax.experimental import pallas as pl
from jax.experimental.layout import Layout, with_layout_constraint
from jax.sharding import PartitionSpec as P

ITERS = 6
HIGHEST = lax.Precision.HIGHEST


def passed_along(array, axis, by):
    size = lax.axis_size(axis)
    pairs = [(i, i + by) for i in range(size) if 0 <= i + by < size]
    return lax.ppermute(array, axis, pairs)


def swapped(value, axis, mask):
    size = lax.axis_size(axis)
    return lax.ppermute(value, axis, [(i, i ^ mask) for i in range(size)])


def summed(value, axis):
    size = lax.axis_size(axis)
    if size & (size - 1):
        return lax.psum(value, axis)
    bit = 1
    while bit < size:
        if bit * 4 <= size:
            near = swapped(value, axis, bit)
            mid = swapped(value, axis, 2 * bit)
            far = swapped(value, axis, 3 * bit)
            value = (value + near) + (mid + far)
            bit *= 4
        else:
            value = value + swapped(value, axis, bit)
            bit *= 2
    return value


def orthonormal(image):
    gram = jnp.einsum("swk,swl->skl", image, image, precision=HIGHEST)
    factor = jnp.linalg.cholesky(gram)
    solved = jax.vmap(lambda fac, rhs: jax.scipy.linalg.solve_triangular(fac, rhs, lower=True))(
        factor, jnp.swapaxes(image, 1, 2)
    )
    return jnp.swapaxes(solved, 1, 2)


def pieces(value):
    high = lax.reduce_precision(value, exponent_bits=8, mantissa_bits=7)
    rest = value - high
    mid = lax.reduce_precision(rest, exponent_bits=8, mantissa_bits=7)
    low = rest - mid
    return high.astype(jnp.bfloat16), mid.astype(jnp.bfloat16), low.astype(jnp.bfloat16)


def thirds(value):
    width = value.shape[1] // 3
    return (value[:, :width] + value[:, width : 2 * width]) + value[:, 2 * width :]


def product(left, right):
    l1, l2, l3 = pieces(left)
    r1, r2, r3 = pieces(right)
    lhs = jnp.concatenate([l1, l1, l2, l1, l2, l3], 1)
    rhs = jnp.concatenate([r1, r2, r1, r3, r2, r1], 1)
    return lax.dot_general(lhs, rhs, (((1,), (1,)), ((), ())), preferred_element_type=jnp.float32)


def _times_kernel(rows_ref, right_ref, out_ref):
    out_ref[...] = jnp.dot(rows_ref[...], right_ref[...], preferred_element_type=jnp.float32)


def times(rows, right, block=512):
    count, inner = rows.shape
    width = right.shape[1]
    return pl.pallas_call(
        _times_kernel,
        grid=(count // block,),
        in_specs=[pl.BlockSpec((block, inner), lambda i: (i, 0)), pl.BlockSpec((inner, width), lambda i: (0, 0))],
        out_specs=pl.BlockSpec((block, width), lambda i: (i, 0)),
        out_shape=jax.ShapeDtypeStruct((count, width), jnp.float32),
    )(rows, right)


def widened(basis, half_cols):
    pad = jnp.zeros((half_cols, basis.shape[2]), basis.dtype)
    first = jnp.concatenate([basis[0], pad], axis=0)
    second = jnp.concatenate([pad, basis[1]], axis=0)
    return jnp.concatenate([first, second], axis=1)


def shards(dosage, tail, missing, start):
    win_count = lax.axis_size("win")
    position = lax.axis_index("win")
    columns = dosage.shape[1]
    half_cols = columns // 2
    comps = start.shape[2]
    total = dosage.shape[0] * lax.axis_size("ind")
    received = passed_along(dosage[:, :half_cols], "win", -1)
    following = jnp.where(position == win_count - 1, tail, received)
    region = jnp.concatenate([dosage, following], axis=1)
    regionf = region.astype(jnp.float32)
    stats = summed(jnp.stack([jnp.sum(regionf, axis=0), jnp.sum(regionf * regionf, axis=0)]), "ind")
    mean = stats[0] / total
    var = stats[1] / total - mean * mean
    miss_here = lax.dynamic_slice_in_dim(missing, position * columns, columns + half_cols)
    weight = jnp.sqrt((total - miss_here.astype(jnp.float32)) / total)
    stand = ((regionf - mean) / jnp.sqrt(var + 1e-05) * weight).astype(jnp.bfloat16)
    stand = with_layout_constraint(stand, Layout(major_to_minor=(0, 1)))

    def project(basis):
        wide = widened(basis, half_cols)
        return thirds(times(stand, jnp.concatenate(pieces(wide), 1)))

    def image_of(basis):
        proj = project(basis)
        split = jnp.concatenate(pieces(proj), 1)
        back = thirds(lax.dot_general(stand, split, (((0,), (0,)), ((), ())), preferred_element_type=jnp.float32))
        parts = jnp.stack([back[:columns, :comps], back[half_cols:, comps:]], 0)
        return summed(parts, "ind") / total

    basis = lax.fori_loop(0, ITERS, lambda step, basis: orthonormal(image_of(basis)), start)
    proj = project(basis)
    variances = summed(jnp.sum(proj * proj, axis=0), "ind").reshape(2, comps) / total
    first = stand[:, :columns].astype(jnp.float32) - product(proj[:, :comps], basis[0])
    second = stand[:, half_cols:].astype(jnp.float32) - product(proj[:, comps:], basis[1])
    scores = jnp.stack([jnp.sum(first * first, axis=1), jnp.sum(second * second, axis=1)], 1) / columns
    return (basis, variances, scores)


def solution(mesh):
    in_specs = (P("ind", "win"), P("ind", None), P(), P("win", None, None))
    out_specs = (P("win", None, None), P("win", None), P("ind", "win"))
    return jax.shard_map(shards, mesh=mesh, in_specs=in_specs, out_specs=out_specs, check_vma=False)
```

```python
import jax
import jax.numpy as jnp
from jax import lax
from jax.experimental.layout import Layout, with_layout_constraint
from jax.sharding import PartitionSpec as P

ITERS = 6
HIGHEST = lax.Precision.HIGHEST


def passed_along(array, axis, by):
    size = lax.axis_size(axis)
    pairs = [(i, i + by) for i in range(size) if 0 <= i + by < size]
    return lax.ppermute(array, axis, pairs)


def swapped(value, axis, mask):
    size = lax.axis_size(axis)
    return lax.ppermute(value, axis, [(i, i ^ mask) for i in range(size)])


def summed(value, axis):
    size = lax.axis_size(axis)
    if size & (size - 1):
        return lax.psum(value, axis)
    levels = size.bit_length() - 1
    bit = 1
    if levels % 2:
        value = value + swapped(value, axis, size // 2)
    while bit * 4 <= size:
        near = swapped(value, axis, bit)
        mid = swapped(value, axis, 2 * bit)
        far = swapped(value, axis, 3 * bit)
        value = (value + near) + (mid + far)
        bit *= 4
    return value


def orthonormal(image):
    gram = jnp.einsum("swk,swl->skl", image, image, precision=HIGHEST)
    factor = jnp.linalg.cholesky(gram)
    solved = jax.vmap(lambda fac, rhs: jax.scipy.linalg.solve_triangular(fac, rhs, lower=True))(
        factor, jnp.swapaxes(image, 1, 2)
    )
    return jnp.swapaxes(solved, 1, 2)


def pieces(value):
    high = lax.reduce_precision(value, exponent_bits=8, mantissa_bits=7)
    rest = value - high
    mid = lax.reduce_precision(rest, exponent_bits=8, mantissa_bits=7)
    low = rest - mid
    return high.astype(jnp.bfloat16), mid.astype(jnp.bfloat16), low.astype(jnp.bfloat16)


def thirds(value):
    width = value.shape[1] // 3
    return (value[:, :width] + value[:, width : 2 * width]) + value[:, 2 * width :]


def product(left, right):
    l1, l2, l3 = pieces(left)
    r1, r2, r3 = pieces(right)
    lhs = jnp.concatenate([l1, l1, l2, l1, l2, l3], 1)
    rhs = jnp.concatenate([r1, r2, r1, r3, r2, r1], 1)
    return lax.dot_general(lhs, rhs, (((1,), (1,)), ((), ())), preferred_element_type=jnp.float32)


def widened(basis, half_cols):
    pad = jnp.zeros((half_cols, basis.shape[2]), basis.dtype)
    first = jnp.concatenate([basis[0], pad], axis=0)
    second = jnp.concatenate([pad, basis[1]], axis=0)
    return jnp.concatenate([first, second], axis=1)


def shards(dosage, tail, missing, start):
    win_count = lax.axis_size("win")
    position = lax.axis_index("win")
    columns = dosage.shape[1]
    half_cols = columns // 2
    comps = start.shape[2]
    total = dosage.shape[0] * lax.axis_size("ind")
    received = passed_along(dosage[:, :half_cols], "win", -1)
    following = jnp.where(position == win_count - 1, tail, received)
    region = jnp.concatenate([dosage, following], axis=1)
    regionf = region.astype(jnp.float32)
    stats = summed(jnp.stack([jnp.sum(regionf, axis=0), jnp.sum(regionf * regionf, axis=0)]), "ind")
    mean = stats[0] / total
    var = stats[1] / total - mean * mean
    miss_here = lax.dynamic_slice_in_dim(missing, position * columns, columns + half_cols)
    weight = jnp.sqrt((total - miss_here.astype(jnp.float32)) / total)
    stand = ((regionf - mean) / jnp.sqrt(var + 1e-05) * weight).astype(jnp.bfloat16)
    stand = with_layout_constraint(stand, Layout(major_to_minor=(0, 1)))

    def project(basis):
        wide = widened(basis, half_cols)
        return thirds(jnp.dot(stand, jnp.concatenate(pieces(wide), 1), preferred_element_type=jnp.float32))

    def image_of(basis):
        proj = project(basis)
        split = jnp.concatenate(pieces(proj), 1)
        back = thirds(lax.dot_general(stand, split, (((0,), (0,)), ((), ())), preferred_element_type=jnp.float32))
        parts = jnp.stack([back[:columns, :comps], back[half_cols:, comps:]], 0)
        return summed(parts, "ind") / total

    basis = lax.fori_loop(0, ITERS, lambda step, basis: orthonormal(image_of(basis)), start)
    proj = project(basis)
    variances = summed(jnp.sum(proj * proj, axis=0), "ind").reshape(2, comps) / total
    first = stand[:, :columns].astype(jnp.float32) - product(proj[:, :comps], basis[0])
    second = stand[:, half_cols:].astype(jnp.float32) - product(proj[:, comps:], basis[1])
    scores = jnp.stack([jnp.sum(first * first, axis=1), jnp.sum(second * second, axis=1)], 1) / columns
    return (basis, variances, scores)


def solution(mesh):
    in_specs = (P("ind", "win"), P("ind", None), P(), P("win", None, None))
    out_specs = (P("win", None, None), P("win", None), P("ind", "win"))
    return jax.shard_map(shards, mesh=mesh, in_specs=in_specs, out_specs=out_specs, check_vma=False)
```

```python
import jax
import jax.numpy as jnp
from jax import lax
from jax.experimental.layout import Layout, with_layout_constraint
from jax.sharding import PartitionSpec as P

ITERS = 6
HIGHEST = lax.Precision.HIGHEST


def passed_along(array, axis, by):
    size = lax.axis_size(axis)
    pairs = [(i, i + by) for i in range(size) if 0 <= i + by < size]
    return lax.ppermute(array, axis, pairs)


def swapped(value, axis, mask):
    size = lax.axis_size(axis)
    return lax.ppermute(value, axis, [(i, i ^ mask) for i in range(size)])


def summed(value, axis):
    size = lax.axis_size(axis)
    if size & (size - 1):
        return lax.psum(value, axis)
    bit = 1
    while bit < size:
        if bit * 4 <= size:
            near = swapped(value, axis, bit)
            mid = swapped(value, axis, 2 * bit)
            far = swapped(value, axis, 3 * bit)
            value = (value + near) + (mid + far)
            bit *= 4
        else:
            value = value + swapped(value, axis, bit)
            bit *= 2
    return value


def orthonormal(image):
    gram = jnp.einsum("swk,swl->skl", image, image, precision=HIGHEST)
    factor = jnp.linalg.cholesky(gram)
    solved = jax.vmap(lambda fac, rhs: jax.scipy.linalg.solve_triangular(fac, rhs, lower=True))(
        factor, jnp.swapaxes(image, 1, 2)
    )
    return jnp.swapaxes(solved, 1, 2)


def pieces(value):
    high = lax.reduce_precision(value, exponent_bits=8, mantissa_bits=7)
    rest = value - high
    mid = lax.reduce_precision(rest, exponent_bits=8, mantissa_bits=7)
    low = rest - mid
    return high.astype(jnp.bfloat16), mid.astype(jnp.bfloat16), low.astype(jnp.bfloat16)


def thirds(value):
    width = value.shape[1] // 3
    return (value[:, :width] + value[:, width : 2 * width]) + value[:, 2 * width :]


def product(left, right):
    l1, l2, l3 = pieces(left)
    r1, r2, r3 = pieces(right)
    lhs = jnp.concatenate([l1, l1, l2, l1, l2, l3], 1)
    rhs = jnp.concatenate([r1, r2, r1, r3, r2, r1], 1)
    return lax.dot_general(lhs, rhs, (((1,), (1,)), ((), ())), preferred_element_type=jnp.float32)


def widened(basis, half_cols):
    pad = jnp.zeros((half_cols, basis.shape[2]), basis.dtype)
    first = jnp.concatenate([basis[0], pad], axis=0)
    second = jnp.concatenate([pad, basis[1]], axis=0)
    return jnp.concatenate([first, second], axis=1)


def shards(dosage, tail, missing, start):
    win_count = lax.axis_size("win")
    position = lax.axis_index("win")
    columns = dosage.shape[1]
    half_cols = columns // 2
    comps = start.shape[2]
    total = dosage.shape[0] * lax.axis_size("ind")
    received = passed_along(dosage[:, :half_cols], "win", -1)
    following = jnp.where(position == win_count - 1, tail, received)
    region = jnp.concatenate([dosage, following], axis=1)
    regionf = region.astype(jnp.float32)
    ownf = dosage.astype(jnp.float32)
    followf = following.astype(jnp.float32)
    own_stats = jnp.stack([jnp.sum(ownf, axis=0), jnp.sum(ownf * ownf, axis=0)])
    follow_stats = jnp.stack([jnp.sum(followf, axis=0), jnp.sum(followf * followf, axis=0)])
    stats = summed(jnp.concatenate([own_stats, follow_stats], axis=1), "ind")
    mean = stats[0] / total
    var = stats[1] / total - mean * mean
    miss_here = lax.dynamic_slice_in_dim(missing, position * columns, columns + half_cols)
    weight = jnp.sqrt((total - miss_here.astype(jnp.float32)) / total)
    stand = ((regionf - mean) / jnp.sqrt(var + 1e-05) * weight).astype(jnp.bfloat16)
    stand = with_layout_constraint(stand, Layout(major_to_minor=(0, 1)))

    def project(basis):
        wide = widened(basis, half_cols)
        return thirds(jnp.dot(stand, jnp.concatenate(pieces(wide), 1), preferred_element_type=jnp.float32))

    def image_of(basis):
        proj = project(basis)
        split = jnp.concatenate(pieces(proj), 1)
        back = thirds(lax.dot_general(stand, split, (((0,), (0,)), ((), ())), preferred_element_type=jnp.float32))
        parts = jnp.stack([back[:columns, :comps], back[half_cols:, comps:]], 0)
        return summed(parts, "ind") / total

    basis = lax.fori_loop(0, ITERS, lambda step, basis: orthonormal(image_of(basis)), start)
    proj = project(basis)
    variances = summed(jnp.sum(proj * proj, axis=0), "ind").reshape(2, comps) / total
    first = stand[:, :columns].astype(jnp.float32) - product(proj[:, :comps], basis[0])
    second = stand[:, half_cols:].astype(jnp.float32) - product(proj[:, comps:], basis[1])
    scores = jnp.stack([jnp.sum(first * first, axis=1), jnp.sum(second * second, axis=1)], 1) / columns
    return (basis, variances, scores)


def solution(mesh):
    in_specs = (P("ind", "win"), P("ind", None), P(), P("win", None, None))
    out_specs = (P("win", None, None), P("win", None), P("ind", "win"))
    return jax.shard_map(shards, mesh=mesh, in_specs=in_specs, out_specs=out_specs, check_vma=False)
```

```python
import jax
import jax.numpy as jnp
from jax import lax
from jax.experimental.layout import Layout, with_layout_constraint
from jax.sharding import PartitionSpec as P

ITERS = 6
HIGHEST = lax.Precision.HIGHEST


def passed_along(array, axis, by):
    size = lax.axis_size(axis)
    pairs = [(i, i + by) for i in range(size) if 0 <= i + by < size]
    return lax.ppermute(array, axis, pairs)


def swapped(value, axis, mask):
    size = lax.axis_size(axis)
    return lax.ppermute(value, axis, [(i, i ^ mask) for i in range(size)])


def summed(value, axis):
    size = lax.axis_size(axis)
    if size & (size - 1):
        return lax.psum(value, axis)
    levels = size.bit_length() - 1
    done = 0
    for low in range(levels):
        if done >> low & 1:
            continue
        high = low + 2
        if high < levels and not done >> high & 1:
            one, two = 1 << low, 1 << high
            near = swapped(value, axis, one)
            mid = swapped(value, axis, two)
            far = swapped(value, axis, one | two)
            value = (value + near) + (mid + far)
            done |= one | two
        else:
            value = value + swapped(value, axis, 1 << low)
            done |= 1 << low
    return value


def orthonormal(image):
    gram = jnp.einsum("swk,swl->skl", image, image, precision=HIGHEST)
    factor = jnp.linalg.cholesky(gram)
    solved = jax.vmap(lambda fac, rhs: jax.scipy.linalg.solve_triangular(fac, rhs, lower=True))(
        factor, jnp.swapaxes(image, 1, 2)
    )
    return jnp.swapaxes(solved, 1, 2)


def pieces(value):
    high = lax.reduce_precision(value, exponent_bits=8, mantissa_bits=7)
    rest = value - high
    mid = lax.reduce_precision(rest, exponent_bits=8, mantissa_bits=7)
    low = rest - mid
    return high.astype(jnp.bfloat16), mid.astype(jnp.bfloat16), low.astype(jnp.bfloat16)


def thirds(value):
    width = value.shape[1] // 3
    return (value[:, :width] + value[:, width : 2 * width]) + value[:, 2 * width :]


def product(left, right):
    l1, l2, l3 = pieces(left)
    r1, r2, r3 = pieces(right)
    lhs = jnp.concatenate([l1, l1, l2, l1, l2, l3], 1)
    rhs = jnp.concatenate([r1, r2, r1, r3, r2, r1], 1)
    return lax.dot_general(lhs, rhs, (((1,), (1,)), ((), ())), preferred_element_type=jnp.float32)


def widened(basis, half_cols):
    pad = jnp.zeros((half_cols, basis.shape[2]), basis.dtype)
    first = jnp.concatenate([basis[0], pad], axis=0)
    second = jnp.concatenate([pad, basis[1]], axis=0)
    return jnp.concatenate([first, second], axis=1)


def shards(dosage, tail, missing, start):
    win_count = lax.axis_size("win")
    position = lax.axis_index("win")
    columns = dosage.shape[1]
    half_cols = columns // 2
    comps = start.shape[2]
    total = dosage.shape[0] * lax.axis_size("ind")
    received = passed_along(dosage[:, :half_cols], "win", -1)
    following = jnp.where(position == win_count - 1, tail, received)
    region = jnp.concatenate([dosage, following], axis=1)
    regionf = region.astype(jnp.float32)
    stats = summed(jnp.stack([jnp.sum(regionf, axis=0), jnp.sum(regionf * regionf, axis=0)]), "ind")
    mean = stats[0] / total
    var = stats[1] / total - mean * mean
    miss_here = lax.dynamic_slice_in_dim(missing, position * columns, columns + half_cols)
    weight = jnp.sqrt((total - miss_here.astype(jnp.float32)) / total)
    stand = ((regionf - mean) / jnp.sqrt(var + 1e-05) * weight).astype(jnp.bfloat16)
    stand = with_layout_constraint(stand, Layout(major_to_minor=(0, 1)))

    def project(basis):
        wide = widened(basis, half_cols)
        return thirds(jnp.dot(stand, jnp.concatenate(pieces(wide), 1), preferred_element_type=jnp.float32))

    def image_of(basis):
        proj = project(basis)
        split = jnp.concatenate(pieces(proj), 1)
        back = thirds(lax.dot_general(stand, split, (((0,), (0,)), ((), ())), preferred_element_type=jnp.float32))
        parts = jnp.stack([back[:columns, :comps], back[half_cols:, comps:]], 0)
        return summed(parts, "ind") / total

    basis = lax.fori_loop(0, ITERS, lambda step, basis: orthonormal(image_of(basis)), start)
    proj = project(basis)
    variances = summed(jnp.sum(proj * proj, axis=0), "ind").reshape(2, comps) / total
    first = stand[:, :columns].astype(jnp.float32) - product(proj[:, :comps], basis[0])
    second = stand[:, half_cols:].astype(jnp.float32) - product(proj[:, comps:], basis[1])
    scores = jnp.stack([jnp.sum(first * first, axis=1), jnp.sum(second * second, axis=1)], 1) / columns
    return (basis, variances, scores)


def solution(mesh):
    in_specs = (P("ind", "win"), P("ind", None), P(), P("win", None, None))
    out_specs = (P("win", None, None), P("win", None), P("ind", "win"))
    return jax.shard_map(shards, mesh=mesh, in_specs=in_specs, out_specs=out_specs, check_vma=False)
```

```python
import jax
import jax.numpy as jnp
from jax import lax
from jax.experimental.layout import Layout, with_layout_constraint
from jax.sharding import PartitionSpec as P

ITERS = 6
HIGHEST = lax.Precision.HIGHEST


def passed_along(array, axis, by):
    size = lax.axis_size(axis)
    pairs = [(i, i + by) for i in range(size) if 0 <= i + by < size]
    return lax.ppermute(array, axis, pairs)


def swapped(value, axis, mask):
    size = lax.axis_size(axis)
    return lax.ppermute(value, axis, [(i, i ^ mask) for i in range(size)])


def summed(value, axis):
    size = lax.axis_size(axis)
    if size & (size - 1):
        return lax.psum(value, axis)
    bit = 1
    while bit < size:
        if bit * 4 <= size:
            near = swapped(value, axis, bit)
            mid = swapped(value, axis, 2 * bit)
            far = swapped(value, axis, 3 * bit)
            value = (value + near) + (mid + far)
            bit *= 4
        else:
            value = value + swapped(value, axis, bit)
            bit *= 2
    return value


def orthonormal(image):
    gram = jnp.einsum("swk,swl->skl", image, image, precision=HIGHEST)
    size = gram.shape[1]
    index = jnp.arange(size)
    factor = jnp.zeros_like(gram)
    for k in range(size):
        column = jnp.where(index >= k, gram[:, :, k] / jnp.sqrt(gram[:, k, k])[:, None], 0.0)
        factor = factor + column[:, :, None] * (index == k)[None, None, :]
        gram = gram - column[:, :, None] * column[:, None, :]
    inverse = jnp.zeros_like(factor)
    rest = jnp.broadcast_to(jnp.eye(size, dtype=factor.dtype), factor.shape)
    for k in range(size):
        row = rest[:, k, :] / factor[:, k, k][:, None]
        inverse = inverse + (index == k)[None, :, None] * row[:, None, :]
        rest = rest - factor[:, :, k][:, :, None] * row[:, None, :]
    return jnp.einsum("swk,sck->swc", image, inverse, precision=HIGHEST)


def pieces(value):
    high = lax.reduce_precision(value, exponent_bits=8, mantissa_bits=7)
    rest = value - high
    mid = lax.reduce_precision(rest, exponent_bits=8, mantissa_bits=7)
    low = rest - mid
    return high.astype(jnp.bfloat16), mid.astype(jnp.bfloat16), low.astype(jnp.bfloat16)


def thirds(value):
    width = value.shape[1] // 3
    return (value[:, :width] + value[:, width : 2 * width]) + value[:, 2 * width :]


def product(left, right):
    l1, l2, l3 = pieces(left)
    r1, r2, r3 = pieces(right)
    lhs = jnp.concatenate([l1, l1, l2, l1, l2, l3], 1)
    rhs = jnp.concatenate([r1, r2, r1, r3, r2, r1], 1)
    return lax.dot_general(lhs, rhs, (((1,), (1,)), ((), ())), preferred_element_type=jnp.float32)


def widened(basis, half_cols):
    pad = jnp.zeros((half_cols, basis.shape[2]), basis.dtype)
    first = jnp.concatenate([basis[0], pad], axis=0)
    second = jnp.concatenate([pad, basis[1]], axis=0)
    return jnp.concatenate([first, second], axis=1)


def shards(dosage, tail, missing, start):
    win_count = lax.axis_size("win")
    position = lax.axis_index("win")
    columns = dosage.shape[1]
    half_cols = columns // 2
    comps = start.shape[2]
    total = dosage.shape[0] * lax.axis_size("ind")
    received = passed_along(dosage[:, :half_cols], "win", -1)
    following = jnp.where(position == win_count - 1, tail, received)
    region = jnp.concatenate([dosage, following], axis=1)
    regionf = region.astype(jnp.float32)
    stats = summed(jnp.stack([jnp.sum(regionf, axis=0), jnp.sum(regionf * regionf, axis=0)]), "ind")
    mean = stats[0] / total
    var = stats[1] / total - mean * mean
    miss_here = lax.dynamic_slice_in_dim(missing, position * columns, columns + half_cols)
    weight = jnp.sqrt((total - miss_here.astype(jnp.float32)) / total)
    stand = ((regionf - mean) / jnp.sqrt(var + 1e-05) * weight).astype(jnp.bfloat16)
    stand = with_layout_constraint(stand, Layout(major_to_minor=(0, 1)))

    def project(basis):
        wide = widened(basis, half_cols)
        return thirds(jnp.dot(stand, jnp.concatenate(pieces(wide), 1), preferred_element_type=jnp.float32))

    def image_of(basis):
        proj = project(basis)
        split = jnp.concatenate(pieces(proj), 1)
        back = thirds(lax.dot_general(stand, split, (((0,), (0,)), ((), ())), preferred_element_type=jnp.float32))
        parts = jnp.stack([back[:columns, :comps], back[half_cols:, comps:]], 0)
        return summed(parts, "ind") / total

    basis = lax.fori_loop(0, ITERS, lambda step, basis: orthonormal(image_of(basis)), start)
    proj = project(basis)
    variances = summed(jnp.sum(proj * proj, axis=0), "ind").reshape(2, comps) / total
    first = stand[:, :columns].astype(jnp.float32) - product(proj[:, :comps], basis[0])
    second = stand[:, half_cols:].astype(jnp.float32) - product(proj[:, comps:], basis[1])
    scores = jnp.stack([jnp.sum(first * first, axis=1), jnp.sum(second * second, axis=1)], 1) / columns
    return (basis, variances, scores)


def solution(mesh):
    in_specs = (P("ind", "win"), P("ind", None), P(), P("win", None, None))
    out_specs = (P("win", None, None), P("win", None), P("ind", "win"))
    return jax.shard_map(shards, mesh=mesh, in_specs=in_specs, out_specs=out_specs, check_vma=False)
```

```python
import jax
import jax.numpy as jnp
from jax import lax
from jax.experimental.layout import Layout, with_layout_constraint
from jax.sharding import PartitionSpec as P

ITERS = 6
HIGHEST = lax.Precision.HIGHEST


def passed_along(array, axis, by):
    size = lax.axis_size(axis)
    pairs = [(i, i + by) for i in range(size) if 0 <= i + by < size]
    return lax.ppermute(array, axis, pairs)


def swapped(value, axis, mask):
    size = lax.axis_size(axis)
    return lax.ppermute(value, axis, [(i, i ^ mask) for i in range(size)])


def summed(value, axis):
    size = lax.axis_size(axis)
    if size & (size - 1):
        return lax.psum(value, axis)
    bit = 1
    while bit < size:
        if bit * 4 <= size:
            near = swapped(value, axis, bit)
            mid = swapped(value, axis, 2 * bit)
            far = swapped(value, axis, 3 * bit)
            value = (value + near) + (mid + far)
            bit *= 4
        else:
            value = value + swapped(value, axis, bit)
            bit *= 2
    return value


def orthonormal(image):
    gram = jnp.einsum("swk,swl->skl", image, image, precision=HIGHEST)
    factor = jnp.linalg.cholesky(gram)
    solved = jax.vmap(lambda fac, rhs: jax.scipy.linalg.solve_triangular(fac, rhs, lower=True))(
        factor, jnp.swapaxes(image, 1, 2)
    )
    return jnp.swapaxes(solved, 1, 2)


def pieces(value):
    high = lax.reduce_precision(value, exponent_bits=8, mantissa_bits=7)
    rest = value - high
    mid = lax.reduce_precision(rest, exponent_bits=8, mantissa_bits=7)
    low = rest - mid
    return high.astype(jnp.bfloat16), mid.astype(jnp.bfloat16), low.astype(jnp.bfloat16)


def thirds(value):
    width = value.shape[1] // 3
    return (value[:, :width] + value[:, width : 2 * width]) + value[:, 2 * width :]


def product(left, right):
    l1, l2, l3 = pieces(left)
    r1, r2, r3 = pieces(right)
    lhs = jnp.concatenate([l1, l1, l2, l1, l2, l3], 1)
    rhs = jnp.concatenate([r1, r2, r1, r3, r2, r1], 1)
    return lax.dot_general(lhs, rhs, (((1,), (1,)), ((), ())), preferred_element_type=jnp.float32)


def widened(basis, half_cols):
    pad = jnp.zeros((half_cols, basis.shape[2]), basis.dtype)
    first = jnp.concatenate([basis[0], pad], axis=0)
    second = jnp.concatenate([pad, basis[1]], axis=0)
    return jnp.concatenate([first, second], axis=1)


def shards(dosage, tail, missing, start):
    win_count = lax.axis_size("win")
    position = lax.axis_index("win")
    columns = dosage.shape[1]
    half_cols = columns // 2
    comps = start.shape[2]
    total = dosage.shape[0] * lax.axis_size("ind")
    received = passed_along(dosage[:, :half_cols], "win", -1)
    following = jnp.where(position == win_count - 1, tail, received)
    region = jnp.concatenate([dosage, following], axis=1)
    regionf = region.astype(jnp.float32)
    ownf = jnp.concatenate([dosage, tail], axis=1).astype(jnp.float32)
    reduced = summed(jnp.stack([jnp.sum(ownf, axis=0), jnp.sum(ownf * ownf, axis=0)]), "ind")
    from_next = passed_along(reduced[:, :half_cols], "win", -1)
    follow_stats = jnp.where(position == win_count - 1, reduced[:, columns:], from_next)
    stats = jnp.concatenate([reduced[:, :columns], follow_stats], axis=1)
    mean = stats[0] / total
    var = stats[1] / total - mean * mean
    miss_here = lax.dynamic_slice_in_dim(missing, position * columns, columns + half_cols)
    weight = jnp.sqrt((total - miss_here.astype(jnp.float32)) / total)
    stand = ((regionf - mean) / jnp.sqrt(var + 1e-05) * weight).astype(jnp.bfloat16)
    stand = with_layout_constraint(stand, Layout(major_to_minor=(0, 1)))

    def project(basis):
        wide = widened(basis, half_cols)
        return thirds(jnp.dot(stand, jnp.concatenate(pieces(wide), 1), preferred_element_type=jnp.float32))

    def image_of(basis):
        proj = project(basis)
        split = jnp.concatenate(pieces(proj), 1)
        back = thirds(lax.dot_general(stand, split, (((0,), (0,)), ((), ())), preferred_element_type=jnp.float32))
        parts = jnp.stack([back[:columns, :comps], back[half_cols:, comps:]], 0)
        return summed(parts, "ind") / total

    basis = lax.fori_loop(0, ITERS, lambda step, basis: orthonormal(image_of(basis)), start)
    proj = project(basis)
    variances = summed(jnp.sum(proj * proj, axis=0), "ind").reshape(2, comps) / total
    first = stand[:, :columns].astype(jnp.float32) - product(proj[:, :comps], basis[0])
    second = stand[:, half_cols:].astype(jnp.float32) - product(proj[:, comps:], basis[1])
    scores = jnp.stack([jnp.sum(first * first, axis=1), jnp.sum(second * second, axis=1)], 1) / columns
    return (basis, variances, scores)


def solution(mesh):
    in_specs = (P("ind", "win"), P("ind", None), P(), P("win", None, None))
    out_specs = (P("win", None, None), P("win", None), P("ind", "win"))
    return jax.shard_map(shards, mesh=mesh, in_specs=in_specs, out_specs=out_specs, check_vma=False)
```

```python
import jax
import jax.numpy as jnp
from jax import lax
from jax.experimental.layout import Layout, with_layout_constraint
from jax.sharding import PartitionSpec as P

ITERS = 6
HIGHEST = lax.Precision.HIGHEST


def passed_along(array, axis, by):
    size = lax.axis_size(axis)
    pairs = [(i, i + by) for i in range(size) if 0 <= i + by < size]
    return lax.ppermute(array, axis, pairs)


def swapped(value, axis, mask):
    size = lax.axis_size(axis)
    return lax.ppermute(value, axis, [(i, i ^ mask) for i in range(size)])


def summed(value, axis):
    size = lax.axis_size(axis)
    if size & (size - 1):
        return lax.psum(value, axis)
    bit = 1
    while bit < size:
        if bit * 4 <= size:
            near = swapped(value, axis, bit)
            mid = swapped(value, axis, 2 * bit)
            far = swapped(value, axis, 3 * bit)
            value = (value + near) + (mid + far)
            bit *= 4
        else:
            value = value + swapped(value, axis, bit)
            bit *= 2
    return value


def orthonormal(image):
    gram = jnp.einsum("swk,swl->skl", image, image, precision=HIGHEST)
    factor = jnp.linalg.cholesky(gram)
    solved = jax.vmap(lambda fac, rhs: jax.scipy.linalg.solve_triangular(fac, rhs, lower=True))(
        factor, jnp.swapaxes(image, 1, 2)
    )
    return jnp.swapaxes(solved, 1, 2)


def pieces(value):
    high = lax.reduce_precision(value, exponent_bits=8, mantissa_bits=7)
    rest = value - high
    mid = lax.reduce_precision(rest, exponent_bits=8, mantissa_bits=7)
    low = rest - mid
    return high.astype(jnp.bfloat16), mid.astype(jnp.bfloat16), low.astype(jnp.bfloat16)


def thirds(value):
    width = value.shape[1] // 3
    return (value[:, :width] + value[:, width : 2 * width]) + value[:, 2 * width :]


def product(left, right):
    l1, l2, l3 = pieces(left)
    r1, r2, r3 = pieces(right)
    lhs = jnp.concatenate([l1, l1, l2, l1, l2, l3], 1)
    rhs = jnp.concatenate([r1, r2, r1, r3, r2, r1], 1)
    return lax.dot_general(lhs, rhs, (((1,), (1,)), ((), ())), preferred_element_type=jnp.float32)


def widened(basis, half_cols):
    pad = jnp.zeros((half_cols, basis.shape[2]), basis.dtype)
    first = jnp.concatenate([basis[0], pad], axis=0)
    second = jnp.concatenate([pad, basis[1]], axis=0)
    return jnp.concatenate([first, second], axis=1)


def shards(dosage, tail, missing, start):
    win_count = lax.axis_size("win")
    position = lax.axis_index("win")
    columns = dosage.shape[1]
    half_cols = columns // 2
    comps = start.shape[2]
    total = dosage.shape[0] * lax.axis_size("ind")
    outgoing = jnp.where(position == 0, tail, dosage[:, :half_cols])
    following = lax.ppermute(outgoing, "win", [(i, (i - 1) % win_count) for i in range(win_count)])
    region = jnp.concatenate([dosage, following], axis=1)
    regionf = region.astype(jnp.float32)
    ownf = jnp.concatenate([dosage, tail], axis=1).astype(jnp.float32)
    reduced = summed(jnp.stack([jnp.sum(ownf, axis=0), jnp.sum(ownf * ownf, axis=0)]), "ind")
    from_next = passed_along(reduced[:, :half_cols], "win", -1)
    follow_stats = jnp.where(position == win_count - 1, reduced[:, columns:], from_next)
    stats = jnp.concatenate([reduced[:, :columns], follow_stats], axis=1)
    mean = stats[0] / total
    var = stats[1] / total - mean * mean
    miss_here = lax.dynamic_slice_in_dim(missing, position * columns, columns + half_cols)
    weight = jnp.sqrt((total - miss_here.astype(jnp.float32)) / total)
    stand = ((regionf - mean) / jnp.sqrt(var + 1e-05) * weight).astype(jnp.bfloat16)
    stand = with_layout_constraint(stand, Layout(major_to_minor=(0, 1)))

    def project(basis):
        wide = widened(basis, half_cols)
        return thirds(jnp.dot(stand, jnp.concatenate(pieces(wide), 1), preferred_element_type=jnp.float32))

    def image_of(basis):
        proj = project(basis)
        split = jnp.concatenate(pieces(proj), 1)
        back = thirds(lax.dot_general(stand, split, (((0,), (0,)), ((), ())), preferred_element_type=jnp.float32))
        parts = jnp.stack([back[:columns, :comps], back[half_cols:, comps:]], 0)
        return summed(parts, "ind") / total

    basis = lax.fori_loop(0, ITERS, lambda step, basis: orthonormal(image_of(basis)), start)
    proj = project(basis)
    variances = summed(jnp.sum(proj * proj, axis=0), "ind").reshape(2, comps) / total
    first = stand[:, :columns].astype(jnp.float32) - product(proj[:, :comps], basis[0])
    second = stand[:, half_cols:].astype(jnp.float32) - product(proj[:, comps:], basis[1])
    scores = jnp.stack([jnp.sum(first * first, axis=1), jnp.sum(second * second, axis=1)], 1) / columns
    return (basis, variances, scores)


def solution(mesh):
    in_specs = (P("ind", "win"), P("ind", None), P(), P("win", None, None))
    out_specs = (P("win", None, None), P("win", None), P("ind", "win"))
    return jax.shard_map(shards, mesh=mesh, in_specs=in_specs, out_specs=out_specs, check_vma=False)
```

```python
import jax
import jax.numpy as jnp
from jax import lax
from jax.experimental.layout import Layout, with_layout_constraint
from jax.sharding import PartitionSpec as P

ITERS = 6
HIGHEST = lax.Precision.HIGHEST


def passed_along(array, axis, by):
    size = lax.axis_size(axis)
    pairs = [(i, i + by) for i in range(size) if 0 <= i + by < size]
    return lax.ppermute(array, axis, pairs)


def swapped(value, axis, mask):
    size = lax.axis_size(axis)
    return lax.ppermute(value, axis, [(i, i ^ mask) for i in range(size)])


def summed(value, axis):
    size = lax.axis_size(axis)
    if size & (size - 1):
        return lax.psum(value, axis)
    bit = 1
    while bit < size:
        if bit * 4 <= size:
            near = swapped(value, axis, bit)
            mid = swapped(value, axis, 2 * bit)
            far = swapped(value, axis, 3 * bit)
            value = (value + near) + (mid + far)
            bit *= 4
        else:
            value = value + swapped(value, axis, bit)
            bit *= 2
    return value


def orthonormal(image):
    gram = jnp.einsum("swk,swl->skl", image, image, precision=HIGHEST)
    factor = jnp.linalg.cholesky(gram)
    solved = jax.vmap(lambda fac, rhs: jax.scipy.linalg.solve_triangular(fac, rhs, lower=True))(
        factor, jnp.swapaxes(image, 1, 2)
    )
    return jnp.swapaxes(solved, 1, 2)


def pieces(value):
    high = lax.reduce_precision(value, exponent_bits=8, mantissa_bits=7)
    rest = value - high
    mid = lax.reduce_precision(rest, exponent_bits=8, mantissa_bits=7)
    low = rest - mid
    return high.astype(jnp.bfloat16), mid.astype(jnp.bfloat16), low.astype(jnp.bfloat16)


def thirds(value):
    width = value.shape[1] // 3
    return (value[:, :width] + value[:, width : 2 * width]) + value[:, 2 * width :]


def product(left, right):
    l1, l2, l3 = pieces(left)
    r1, r2, r3 = pieces(right)
    lhs = jnp.concatenate([l1, l1, l2, l1, l2, l3], 1)
    rhs = jnp.concatenate([r1, r2, r1, r3, r2, r1], 1)
    return lax.dot_general(lhs, rhs, (((1,), (1,)), ((), ())), preferred_element_type=jnp.float32)


def widened(basis, half_cols):
    pad = jnp.zeros((half_cols, basis.shape[2]), basis.dtype)
    first = jnp.concatenate([basis[0], pad], axis=0)
    second = jnp.concatenate([pad, basis[1]], axis=0)
    return jnp.concatenate([first, second], axis=1)


def shards(dosage, tail, missing, start):
    win_count = lax.axis_size("win")
    position = lax.axis_index("win")
    columns = dosage.shape[1]
    half_cols = columns // 2
    comps = start.shape[2]
    total = dosage.shape[0] * lax.axis_size("ind")
    received = passed_along(dosage[:, :half_cols], "win", -1)
    following = jnp.where(position == win_count - 1, tail, received)
    region = jnp.concatenate([dosage, following], axis=1)
    regionf = region.astype(jnp.float32)
    ownf = jnp.concatenate([dosage, tail], axis=1).astype(jnp.float32)
    reduced = summed(jnp.stack([jnp.sum(ownf, axis=0), jnp.sum(ownf * ownf, axis=0)]), "ind")
    from_next = passed_along(reduced[:, :half_cols], "win", -1)
    follow_stats = jnp.where(position == win_count - 1, reduced[:, columns:], from_next)
    stats = jnp.concatenate([reduced[:, :columns], follow_stats], axis=1)
    mean = stats[0] / total
    var = stats[1] / total - mean * mean
    miss_here = lax.dynamic_slice_in_dim(missing, position * columns, columns + half_cols)
    weight = jnp.sqrt((total - miss_here.astype(jnp.float32)) / total)
    stand = ((regionf - mean) / jnp.sqrt(var + 1e-05) * weight).astype(jnp.bfloat16)
    stand = with_layout_constraint(stand, Layout(major_to_minor=(0, 1)))

    def project(basis):
        wide = widened(basis, half_cols)
        return thirds(jnp.dot(stand, jnp.concatenate(pieces(wide), 1), preferred_element_type=jnp.float32))

    def image_of(basis):
        proj = project(basis)
        split = jnp.concatenate(pieces(proj), 1)
        back = thirds(lax.dot_general(stand, split, (((0,), (0,)), ((), ())), preferred_element_type=jnp.float32))
        parts = jnp.stack([back[:columns, :comps], back[half_cols:, comps:]], 0)
        return summed(parts, "ind") / total

    basis = lax.fori_loop(0, ITERS, lambda step, basis: orthonormal(image_of(basis)), start, unroll=2)
    proj = project(basis)
    variances = summed(jnp.sum(proj * proj, axis=0), "ind").reshape(2, comps) / total
    first = stand[:, :columns].astype(jnp.float32) - product(proj[:, :comps], basis[0])
    second = stand[:, half_cols:].astype(jnp.float32) - product(proj[:, comps:], basis[1])
    scores = jnp.stack([jnp.sum(first * first, axis=1), jnp.sum(second * second, axis=1)], 1) / columns
    return (basis, variances, scores)


def solution(mesh):
    in_specs = (P("ind", "win"), P("ind", None), P(), P("win", None, None))
    out_specs = (P("win", None, None), P("win", None), P("ind", "win"))
    return jax.shard_map(shards, mesh=mesh, in_specs=in_specs, out_specs=out_specs, check_vma=False)
```

```python
import jax
import jax.numpy as jnp
from jax import lax
from jax.experimental.layout import Layout, with_layout_constraint
from jax.sharding import PartitionSpec as P

ITERS = 6
HIGHEST = lax.Precision.HIGHEST


def passed_along(array, axis, by):
    size = lax.axis_size(axis)
    pairs = [(i, i + by) for i in range(size) if 0 <= i + by < size]
    return lax.ppermute(array, axis, pairs)


def swapped(value, axis, mask):
    size = lax.axis_size(axis)
    return lax.ppermute(value, axis, [(i, i ^ mask) for i in range(size)])


def summed(value, axis):
    size = lax.axis_size(axis)
    if size & (size - 1):
        return lax.psum(value, axis)
    bit = 1
    while bit < size:
        if bit * 4 <= size:
            near = swapped(value, axis, bit)
            mid = swapped(value, axis, 2 * bit)
            far = swapped(value, axis, 3 * bit)
            value = (value + near) + (mid + far)
            bit *= 4
        else:
            value = value + swapped(value, axis, bit)
            bit *= 2
    return value


def orthonormal(image):
    gram = jnp.einsum("swk,swl->skl", image, image, precision=HIGHEST)
    factor = jnp.linalg.cholesky(gram)
    solved = jax.vmap(lambda fac, rhs: jax.scipy.linalg.solve_triangular(fac, rhs, lower=True))(
        factor, jnp.swapaxes(image, 1, 2)
    )
    return jnp.swapaxes(solved, 1, 2)


def pieces(value):
    high = lax.reduce_precision(value, exponent_bits=8, mantissa_bits=7)
    rest = value - high
    mid = lax.reduce_precision(rest, exponent_bits=8, mantissa_bits=7)
    low = rest - mid
    return high.astype(jnp.bfloat16), mid.astype(jnp.bfloat16), low.astype(jnp.bfloat16)


def thirds(value):
    width = value.shape[1] // 3
    return (value[:, :width] + value[:, width : 2 * width]) + value[:, 2 * width :]


def product(left, right):
    l1, l2, l3 = pieces(left)
    r1, r2, r3 = pieces(right)
    lhs = jnp.concatenate([l1, l1, l2, l1, l2, l3], 1)
    rhs = jnp.concatenate([r1, r2, r1, r3, r2, r1], 1)
    return lax.dot_general(lhs, rhs, (((1,), (1,)), ((), ())), preferred_element_type=jnp.float32)


def widened(basis, half_cols):
    pad = jnp.zeros((half_cols, basis.shape[2]), basis.dtype)
    first = jnp.concatenate([basis[0], pad], axis=0)
    second = jnp.concatenate([pad, basis[1]], axis=0)
    return jnp.concatenate([first, second], axis=1)


def shards(dosage, tail, missing, start):
    win_count = lax.axis_size("win")
    position = lax.axis_index("win")
    columns = dosage.shape[1]
    half_cols = columns // 2
    comps = start.shape[2]
    total = dosage.shape[0] * lax.axis_size("ind")
    received = passed_along(dosage[:, :half_cols], "win", -1)
    following = jnp.where(position == win_count - 1, tail, received)
    region = jnp.concatenate([dosage, following], axis=1)
    regionf = region.astype(jnp.float32)
    ownf = jnp.concatenate([dosage, tail], axis=1).astype(jnp.float32)
    reduced = summed(jnp.stack([jnp.sum(ownf, axis=0), jnp.sum(ownf * ownf, axis=0)]), "ind")
    from_next = passed_along(reduced[:, :half_cols], "win", -1)
    follow_stats = jnp.where(position == win_count - 1, reduced[:, columns:], from_next)
    stats = jnp.concatenate([reduced[:, :columns], follow_stats], axis=1)
    mean = stats[0] / total
    var = stats[1] / total - mean * mean
    miss_here = lax.dynamic_slice_in_dim(missing, position * columns, columns + half_cols)
    weight = jnp.sqrt((total - miss_here.astype(jnp.float32)) / total)
    stand = ((regionf - mean) / jnp.sqrt(var + 1e-05) * weight).astype(jnp.bfloat16)
    stand = with_layout_constraint(stand, Layout(major_to_minor=(0, 1)))

    def project(basis):
        wide = widened(basis, half_cols)
        return thirds(jnp.dot(stand, jnp.concatenate(pieces(wide), 1), preferred_element_type=jnp.float32))

    def image_of(basis):
        proj = project(basis)
        split = jnp.concatenate(pieces(proj), 1)
        back = thirds(lax.dot_general(stand, split, (((0,), (0,)), ((), ())), preferred_element_type=jnp.float32))
        back = summed(back, "ind") / total
        return jnp.stack([back[:columns, :comps], back[half_cols:, comps:]], 0)

    basis = lax.fori_loop(0, ITERS, lambda step, basis: orthonormal(image_of(basis)), start)
    proj = project(basis)
    variances = summed(jnp.sum(proj * proj, axis=0), "ind").reshape(2, comps) / total
    first = stand[:, :columns].astype(jnp.float32) - product(proj[:, :comps], basis[0])
    second = stand[:, half_cols:].astype(jnp.float32) - product(proj[:, comps:], basis[1])
    scores = jnp.stack([jnp.sum(first * first, axis=1), jnp.sum(second * second, axis=1)], 1) / columns
    return (basis, variances, scores)


def solution(mesh):
    in_specs = (P("ind", "win"), P("ind", None), P(), P("win", None, None))
    out_specs = (P("win", None, None), P("win", None), P("ind", "win"))
    return jax.shard_map(shards, mesh=mesh, in_specs=in_specs, out_specs=out_specs, check_vma=False)
```
